32 devices in a mesh: groups: 2 (over x), dp: 16 (over z, y, core).
Axes of the slice: x: 2, y: 2, z: 4, core: 2. Of those that a mesh axis runs over, the one named last changes fastest.
Arguments:
- layer_input: bfloat16 [8192, 8192], P(('groups', 'dp')), parts along dimension 0, may hold values from -6 to 6
- grad_values: bfloat16 [8192, 1024], P(('groups', 'dp')), parts along dimension 0, may hold values from -6 to 6
- base_weight: bfloat16 [8192, 1024], P('dp'), may hold values from -0.0625 to 0.0625
- tile_ids: int32 [32], P(('groups', 'dp')), parts along dimension 0, may hold values from 0 to 511, as said below
- tile_delta: bfloat16 [32, 128, 128], P(('groups', 'dp')), parts along dimension 0, may hold values from -0.1875 to 0.1875
Outputs:
- grad_input: bfloat16 [8192, 8192], P(('groups', 'dp')), parts along dimension 0
- grad_tiles: float32 [32, 128, 128], P(('groups', 'dp')), parts along dimension 0
The draws below stay inside these ranges and needn't reach their ends.
There are 2 independent parts, one for each index of `groups`. The reference program is written for one: setup_inputs(seed, part) draws one part's arguments, and reference() takes and returns one part's arrays. A program takes and returns all parts, laid end to end along the dimension named above; an argument that names none is the same for every part. Nothing has to cross between parts.
Inputs may be any that keep to these rules, and one draw needn't show every extreme that they name: `tile_ids`: the 16 tile numbers are distinct; every tile of some tile row is listed.
All inputs are finite; a program needn't handle non-finite values.
Results may differ from the reference program's by a relative error of at most 0.0034.
Values may be sent and summed in bfloat16 or wider, within the bound.
No kernel may reach another device: no remote copies, remote signals or barrier semaphores. Data moves between devices by JAX's collectives and lax.ppermute only.
A program may use at most 128 MiB of HBM per device.

```python
import math
import jax
import jax.numpy as jnp
from jax import lax

D = 8192
KV = 1024
TILE = 128
ROW_TILES = 64
COL_TILES = 8
NT = 512
TOKENS = 4096
LISTED = 16


def draw_tile_ids(key, part):
    key_bias = jax.random.fold_in(key, 11)
    key_hot = jax.random.fold_in(key, 12)
    key_noise = jax.random.fold_in(key, 13)
    panel_bias = jax.random.randint(key_bias, (ROW_TILES,), 0, 4)
    hot_panel = jax.random.randint(key_hot, (), 0, ROW_TILES)
    panel_bias = jnp.where(jnp.arange(ROW_TILES) == hot_panel, 8, panel_bias)
    noise = jax.random.randint(key_noise, (NT,), 0, 4096)
    numbers = jnp.arange(NT)
    score = (panel_bias[numbers // COL_TILES] * 4096 + noise) * NT + numbers
    chosen = lax.top_k(score, LISTED)[1]
    return chosen.astype(jnp.int32)


def steps_of(rng, shape, pieces, low, largest):
    def one(axis_at, shards_of):
        heights = jax.random.uniform(jax.random.fold_in(jax.random.fold_in(rng, 6), axis_at), (shards_of,), jnp.float32, low / len(pieces), largest / len(pieces))
        return jnp.repeat(jnp.exp(heights), shape[axis_at] // shards_of).reshape((-1,) + (1,) * (len(shape) - axis_at - 1))

    factor_of = one(*pieces[0])
    for cut in pieces[1:]:
        factor_of = factor_of * one(*cut)
    return factor_of


def gaussian(rng, shape, spread, reach, pieces=(), kind=jnp.bfloat16):
    result = jax.random.normal(rng, shape, jnp.float32) * spread
    if len(pieces) > 0:
        result = steps_of(rng, shape, pieces, -0.22, 0.18) * result
    return jnp.clip(result, min=-reach, max=reach).astype(kind)


def setup_inputs(seed: int = 0, part: int = 0) -> dict:
    key_list = jax.random.split(jax.random.key(seed), 6)
    own_keys = jax.random.split(jax.random.fold_in(key_list[5], part), 6)
    return {
        "layer_input": gaussian(own_keys[0], (TOKENS, D), 1.0, 6.0, ((0, 16),)),
        "grad_values": gaussian(own_keys[1], (TOKENS, KV), 1.0, 6.0, ((0, 16),)),
        "base_weight": gaussian(key_list[2], (D, KV), D ** -0.5, 0.0625, ((0, 16),)),
        "tile_ids": draw_tile_ids(jax.random.fold_in(jax.random.fold_in(key_list[5], part), 71), part),
        "tile_delta": gaussian(own_keys[4], (LISTED, TILE, TILE), KV ** -0.5, 0.1875, ((0, 16),)),
    }


def delta_matrix(tile_ids, tile_delta):
    tile_rows = tile_ids // COL_TILES
    tile_cols = tile_ids % COL_TILES
    field = jnp.zeros((ROW_TILES, TILE, COL_TILES, TILE), tile_delta.dtype)
    field = field.at[tile_rows, :, tile_cols, :].set(tile_delta)
    return field.reshape(ROW_TILES * TILE, COL_TILES * TILE)

def reference(layer_input, grad_values, base_weight, tile_ids, tile_delta):
    field = delta_matrix(tile_ids, tile_delta)
    merged = (base_weight.astype(jnp.float32) + field.astype(jnp.float32)).astype(jnp.bfloat16)
    grad_input = jnp.dot(grad_values, merged.T, preferred_element_type=jnp.float32).astype(jnp.bfloat16)

    def one_tile(tile_number):
        first_row = (tile_number // COL_TILES).astype(jnp.int32) * TILE
        first_col = (tile_number % COL_TILES).astype(jnp.int32) * TILE
        rows_panel = lax.dynamic_slice_in_dim(layer_input, first_row, TILE, 1)
        cols_panel = lax.dynamic_slice_in_dim(grad_values, first_col, TILE, 1)
        return jnp.dot(rows_panel.T, cols_panel, preferred_element_type=jnp.float32)
    grad_tiles = lax.map(one_tile, tile_ids) * (1.0 / math.sqrt(TOKENS))
    return (grad_input, grad_tiles)
```

```python
import math

import jax
import jax.numpy as jnp
from jax import lax
from jax.experimental import pallas as pl
from jax.experimental.pallas import tpu as pltpu
from jax.sharding import PartitionSpec as P

TILE = 128
BLOCK_ROWS = 1024


def merged_matmul(tile_rows, tile_cols, grad_values, full_base, all_deltas, interpret=False):
    tokens, kv = grad_values.shape
    d_model = full_base.shape[0]
    listed = all_deltas.shape[0]
    col_tiles = kv // TILE
    tiles_per_block = BLOCK_ROWS // TILE

    def kernel(rows_ref, cols_ref, gv_ref, base_ref, delta_ref, out_ref):
        i = pl.program_id(0)

        def patch(j, carry):
            r = rows_ref[j] - i * tiles_per_block

            @pl.when((r >= 0) & (r < tiles_per_block))
            def _():
                c = cols_ref[j]
                rs = pl.ds(pl.multiple_of(r * TILE, TILE), TILE)
                for cc in range(col_tiles):

                    @pl.when(c == cc)
                    def _():
                        cs = slice(cc * TILE, (cc + 1) * TILE)
                        cur = base_ref[rs, cs].astype(jnp.float32)
                        add = delta_ref[j].astype(jnp.float32)
                        base_ref[rs, cs] = (cur + add).astype(jnp.bfloat16)

            return carry

        lax.fori_loop(0, listed, patch, 0)
        out_ref[...] = lax.dot_general(
            gv_ref[...],
            base_ref[...],
            (((1,), (1,)), ((), ())),
            preferred_element_type=jnp.float32,
        ).astype(out_ref.dtype)

    return pl.pallas_call(
        kernel,
        grid_spec=pltpu.PrefetchScalarGridSpec(
            num_scalar_prefetch=2,
            grid=(d_model // BLOCK_ROWS,),
            in_specs=[
                pl.BlockSpec((tokens, kv), lambda i, r, c: (0, 0)),
                pl.BlockSpec((BLOCK_ROWS, kv), lambda i, r, c: (i, 0)),
                pl.BlockSpec((listed, TILE, TILE), lambda i, r, c: (0, 0, 0)),
            ],
            out_specs=pl.BlockSpec((tokens, BLOCK_ROWS), lambda i, r, c: (0, i)),
        ),
        out_shape=jax.ShapeDtypeStruct((tokens, d_model), jnp.bfloat16),
        interpret=interpret,
    )(tile_rows, tile_cols, grad_values, full_base, all_deltas)


def body(layer_input, grad_values, base_weight, tile_ids, tile_delta):
    n = lax.axis_size("dp")
    tokens_here = layer_input.shape[0]
    d_model = layer_input.shape[1]
    kv = grad_values.shape[1]
    row_tiles = d_model // TILE
    col_tiles = kv // TILE

    full_base = lax.all_gather(base_weight, "dp", axis=0, tiled=True)

    all_ids = lax.all_to_all(jnp.broadcast_to(tile_ids, (n,)), "dp", 0, 0, tiled=True)
    all_deltas = lax.all_to_all(
        jnp.broadcast_to(tile_delta, (n, TILE, TILE)), "dp", 0, 0, tiled=True
    )
    tile_rows = all_ids // col_tiles
    tile_cols = all_ids % col_tiles

    input_panels = layer_input.reshape(tokens_here, row_tiles, TILE)
    grad_panels = grad_values.reshape(tokens_here, col_tiles, TILE)
    rows_taken = jnp.take(input_panels, tile_rows, axis=1)
    cols_taken = jnp.take(grad_panels, tile_cols, axis=1)
    partial = jnp.einsum(
        "tja,tjb->jab", rows_taken, cols_taken, preferred_element_type=jnp.float32
    )
    from_each = lax.all_to_all(partial, "dp", 0, 0, tiled=True)
    factor = 1.0 / math.sqrt(tokens_here * n)
    grad_tiles = jnp.sum(from_each, axis=0, keepdims=True) * factor

    grad_input = merged_matmul(tile_rows, tile_cols, grad_values, full_base, all_deltas)
    return (grad_input, grad_tiles)


def solution(mesh):
    placed = (
        P(("groups", "dp"), None),
        P(("groups", "dp"), None),
        P("dp", None),
        P(("groups", "dp")),
        P(("groups", "dp"), None, None),
    )
    return jax.shard_map(
        body,
        mesh=mesh,
        in_specs=placed,
        out_specs=(P(("groups", "dp"), None), P(("groups", "dp"), None, None)),
        check_vma=False,
    )
```

```python
import math

import jax
import jax.numpy as jnp
from jax import lax
from jax.experimental import pallas as pl
from jax.experimental.pallas import tpu as pltpu
from jax.sharding import Mesh
from jax.sharding import PartitionSpec as P

TILE = 128
BLOCK_ROWS = 1024
DP = ("chips", "core")


def merged_matmul(tile_rows, tile_cols, grad_values, gathered, shard, all_deltas, interpret=False):
    tokens, kv = grad_values.shape
    n = gathered.shape[0]
    d_model = n * shard
    listed = all_deltas.shape[0]
    col_tiles = kv // TILE
    block_rows = max(BLOCK_ROWS, shard)
    per_block = block_rows // shard
    tiles_per_block = block_rows // TILE
    piece = min(shard, TILE)

    def kernel(rows_ref, cols_ref, gv_ref, base_ref, delta_ref, out_ref):
        i = pl.program_id(0)

        def patch(j, carry):
            r = rows_ref[j] - i * tiles_per_block

            @pl.when((r >= 0) & (r < tiles_per_block))
            def _():
                c = cols_ref[j]
                for q in range(TILE // piece):
                    at = r * TILE + q * piece
                    si = at // shard
                    rs = pl.ds(pl.multiple_of(at % shard, piece), piece)
                    for cc in range(col_tiles):

                        @pl.when(c == cc)
                        def _():
                            cs = slice(cc * TILE, (cc + 1) * TILE)
                            cur = base_ref[si, rs, cs].astype(jnp.float32)
                            add = delta_ref[j, q * piece:(q + 1) * piece, :].astype(jnp.float32)
                            base_ref[si, rs, cs] = (cur + add).astype(jnp.bfloat16)

            return carry

        lax.fori_loop(0, listed, patch, 0)
        merged = base_ref[...].reshape(block_rows, kv)
        out_ref[...] = lax.dot_general(
            gv_ref[...],
            merged,
            (((1,), (1,)), ((), ())),
            preferred_element_type=jnp.float32,
        ).astype(out_ref.dtype)

    return pl.pallas_call(
        kernel,
        grid_spec=pltpu.PrefetchScalarGridSpec(
            num_scalar_prefetch=2,
            grid=(d_model // block_rows,),
            in_specs=[
                pl.BlockSpec((tokens, kv), lambda i, r, c: (0, 0)),
                pl.BlockSpec((per_block, shard, kv), lambda i, r, c: (i, 0, 0)),
                pl.BlockSpec((listed, TILE, TILE), lambda i, r, c: (0, 0, 0)),
            ],
            out_specs=pl.BlockSpec((tokens, block_rows), lambda i, r, c: (0, i)),
        ),
        out_shape=jax.ShapeDtypeStruct((tokens, d_model), jnp.bfloat16),
        interpret=interpret,
    )(tile_rows, tile_cols, grad_values, gathered, all_deltas)


def body(layer_input, grad_values, base_weight, tile_ids, tile_delta):
    chips = lax.axis_size("chips")
    n = 2 * chips
    tokens_here = layer_input.shape[0]
    d_model = layer_input.shape[1]
    kv = grad_values.shape[1]
    shard = base_weight.shape[0]
    row_tiles = d_model // TILE
    col_tiles = kv // TILE

    packed = jnp.concatenate([base_weight, tile_delta.reshape(-1, kv)], axis=0)
    gathered = lax.all_gather(packed, DP, axis=0, tiled=False)

    all_ids = lax.all_to_all(jnp.broadcast_to(tile_ids, (n,)), DP, 0, 0, tiled=True)
    tile_rows = all_ids // col_tiles
    tile_cols = all_ids % col_tiles

    input_panels = layer_input.reshape(tokens_here, row_tiles, TILE)
    grad_panels = grad_values.reshape(tokens_here, col_tiles, TILE)
    rows_taken = jnp.take(input_panels, tile_rows, axis=1)
    cols_taken = jnp.take(grad_panels, tile_cols, axis=1)
    partial = jnp.einsum(
        "tja,tjb->jab", rows_taken, cols_taken, preferred_element_type=jnp.float32
    ).reshape(chips, 2, TILE, TILE)
    core = lax.axis_index("core")
    mine = lax.dynamic_index_in_dim(partial, core, axis=1, keepdims=False)
    other = lax.dynamic_index_in_dim(partial, 1 - core, axis=1, keepdims=False)
    chip_sum = mine + lax.ppermute(other, "core", [(0, 1), (1, 0)])
    from_chips = lax.all_to_all(chip_sum, "chips", 0, 0, tiled=True)
    factor = 1.0 / math.sqrt(tokens_here * n)
    grad_tiles = jnp.sum(from_chips, axis=0, keepdims=True) * factor

    all_deltas = gathered[:, shard:, :].reshape(n, TILE, TILE)
    grad_input = merged_matmul(
        tile_rows, tile_cols, grad_values, gathered, shard, all_deltas
    )
    return (grad_input, grad_tiles)


def solution(mesh):
    groups, dp = mesh.devices.shape
    split = Mesh(mesh.devices.reshape(groups, dp // 2, 2), ("groups",) + DP)
    tokens = ("groups",) + DP
    placed = (
        P(tokens, None),
        P(tokens, None),
        P(DP, None),
        P(tokens),
        P(tokens, None, None),
    )
    return jax.shard_map(
        body,
        mesh=split,
        in_specs=placed,
        out_specs=(P(tokens, None), P(tokens, None, None)),
        check_vma=False,
    )
```

```python
import math

import jax
import jax.numpy as jnp
from jax import lax
from jax.experimental import pallas as pl
from jax.experimental.pallas import tpu as pltpu
from jax.sharding import Mesh
from jax.sharding import PartitionSpec as P

TILE = 128
BLOCK_ROWS = 4096
DP = ("chips", "core")


def merged_matmul(tile_rows, tile_cols, grad_values, gathered, shard, interpret=False):
    tokens, kv = grad_values.shape
    n, packed_rows, _ = gathered.shape
    sub = packed_rows - shard
    d_model = n * shard
    col_tiles = kv // TILE
    block_rows = max(min(BLOCK_ROWS, d_model), shard)
    per_block = block_rows // shard
    tiles_per_block = block_rows // TILE

    def kernel(rows_ref, cols_ref, gv_ref, base_ref, delta_ref, out_ref):
        i = pl.program_id(0)

        def patch(j, carry):
            r = rows_ref[j] - i * tiles_per_block

            @pl.when((r >= 0) & (r < tiles_per_block))
            def _():
                c = cols_ref[j]
                for a in range(col_tiles):
                    at = r * TILE + a * sub
                    si = at // shard
                    rs = pl.ds(pl.multiple_of(at % shard, sub), sub)
                    add = delta_ref[j, :, a * TILE:(a + 1) * TILE].astype(jnp.float32)
                    for cc in range(col_tiles):

                        @pl.when(c == cc)
                        def _():
                            cs = slice(cc * TILE, (cc + 1) * TILE)
                            cur = base_ref[si, rs, cs].astype(jnp.float32)
                            base_ref[si, rs, cs] = (cur + add).astype(jnp.bfloat16)

            return carry

        lax.fori_loop(0, n, patch, 0)
        merged = base_ref[...].reshape(block_rows, kv)
        out_ref[...] = lax.dot_general(
            gv_ref[...],
            merged,
            (((1,), (1,)), ((), ())),
            preferred_element_type=jnp.float32,
        ).astype(out_ref.dtype)

    return pl.pallas_call(
        kernel,
        grid_spec=pltpu.PrefetchScalarGridSpec(
            num_scalar_prefetch=2,
            grid=(d_model // block_rows,),
            in_specs=[
                pl.BlockSpec((tokens, kv), lambda i, r, c: (0, 0)),
                pl.BlockSpec((per_block, shard, kv), lambda i, r, c: (i, 0, 0)),
                pl.BlockSpec((n, sub, kv), lambda i, r, c: (0, shard // sub, 0)),
            ],
            out_specs=pl.BlockSpec((tokens, block_rows), lambda i, r, c: (0, i)),
        ),
        out_shape=jax.ShapeDtypeStruct((tokens, d_model), jnp.bfloat16),
        interpret=interpret,
    )(tile_rows, tile_cols, grad_values, gathered, gathered)


def body(layer_input, grad_values, base_weight, tile_ids, tile_delta):
    chips = lax.axis_size("chips")
    n = 2 * chips
    tokens_here = layer_input.shape[0]
    d_model = layer_input.shape[1]
    kv = grad_values.shape[1]
    shard = base_weight.shape[0]
    row_tiles = d_model // TILE
    col_tiles = kv // TILE

    sub = TILE * TILE // kv
    delta_rows = tile_delta.reshape(col_tiles, sub, TILE).transpose(1, 0, 2).reshape(sub, kv)
    packed = jnp.concatenate([base_weight, delta_rows], axis=0)
    gathered = lax.all_gather(packed, DP, axis=0, tiled=False)

    all_ids = lax.all_to_all(jnp.broadcast_to(tile_ids, (n,)), DP, 0, 0, tiled=True)
    tile_rows = all_ids // col_tiles
    tile_cols = all_ids % col_tiles

    input_panels = layer_input.reshape(tokens_here, row_tiles, TILE)
    grad_panels = grad_values.reshape(tokens_here, col_tiles, TILE)
    rows_taken = jnp.take(input_panels, tile_rows, axis=1)
    cols_taken = jnp.take(grad_panels, tile_cols, axis=1)
    partial = jnp.einsum(
        "tja,tjb->jab", rows_taken, cols_taken, preferred_element_type=jnp.float32
    ).reshape(chips, 2, TILE, TILE)
    core = lax.axis_index("core")
    mine = lax.dynamic_index_in_dim(partial, core, axis=1, keepdims=False)
    other = lax.dynamic_index_in_dim(partial, 1 - core, axis=1, keepdims=False)
    chip_sum = mine + lax.ppermute(other, "core", [(0, 1), (1, 0)])
    from_chips = lax.all_to_all(chip_sum, "chips", 0, 0, tiled=True)
    factor = 1.0 / math.sqrt(tokens_here * n)
    grad_tiles = jnp.sum(from_chips, axis=0, keepdims=True) * factor

    grad_input = merged_matmul(tile_rows, tile_cols, grad_values, gathered, shard)
    return (grad_input, grad_tiles)


def solution(mesh):
    groups, dp = mesh.devices.shape
    split = Mesh(mesh.devices.reshape(groups, dp // 2, 2), ("groups",) + DP)
    tokens = ("groups",) + DP
    placed = (
        P(tokens, None),
        P(tokens, None),
        P(DP, None),
        P(tokens),
        P(tokens, None, None),
    )
    return jax.shard_map(
        body,
        mesh=split,
        in_specs=placed,
        out_specs=(P(tokens, None), P(tokens, None, None)),
        check_vma=False,
    )
```

```python
import math

import jax
import jax.numpy as jnp
from jax import lax
from jax.experimental import pallas as pl
from jax.experimental.pallas import tpu as pltpu
from jax.sharding import Mesh
from jax.sharding import PartitionSpec as P

TILE = 128
BLOCK_ROWS = 4096
DP = ("chips", "core")


def merged_matmul(tile_rows, tile_cols, own_group, grad_values, gathered, interpret=False):
    tokens, kv = grad_values.shape
    halves, n, packed_rows, _ = gathered.shape
    sub = TILE * TILE // kv
    half = packed_rows - sub
    shard = halves * half
    d_model = n * shard
    col_tiles = kv // TILE
    block_rows = max(min(BLOCK_ROWS, d_model), shard)
    per_block = block_rows // shard
    tiles_per_block = block_rows // TILE

    def kernel(rows_ref, cols_ref, group_ref, gv_ref, base_ref, delta_ref, out_ref):
        i = pl.program_id(0)

        def patch(j, carry):
            r = rows_ref[j] - i * tiles_per_block

            @pl.when((r >= 0) & (r < tiles_per_block))
            def _():
                c = cols_ref[j]
                for a in range(col_tiles):
                    at = r * TILE + a * sub
                    si = at // shard
                    gi = (at % shard) // half
                    rs = pl.ds(pl.multiple_of(at % half, sub), sub)
                    add = delta_ref[0, j, :, a * TILE:(a + 1) * TILE].astype(jnp.float32)
                    for cc in range(col_tiles):

                        @pl.when(c == cc)
                        def _():
                            cs = slice(cc * TILE, (cc + 1) * TILE)
                            cur = base_ref[gi, si, rs, cs].astype(jnp.float32)
                            base_ref[gi, si, rs, cs] = (cur + add).astype(jnp.bfloat16)

            return carry

        lax.fori_loop(0, n, patch, 0)
        for gi in range(halves):
            part = lax.dot_general(
                gv_ref[...],
                base_ref[gi].reshape(per_block * half, kv),
                (((1,), (1,)), ((), ())),
                preferred_element_type=jnp.float32,
            ).astype(out_ref.dtype)
            for si in range(per_block):
                at = si * shard + gi * half
                out_ref[:, at:at + half] = part[:, si * half:(si + 1) * half]

    return pl.pallas_call(
        kernel,
        grid_spec=pltpu.PrefetchScalarGridSpec(
            num_scalar_prefetch=3,
            grid=(d_model // block_rows,),
            in_specs=[
                pl.BlockSpec((tokens, kv), lambda i, r, c, g: (0, 0)),
                pl.BlockSpec((halves, per_block, half, kv), lambda i, r, c, g: (0, i, 0, 0)),
                pl.BlockSpec((1, n, sub, kv), lambda i, r, c, g: (g[0], 0, half // sub, 0)),
            ],
            out_specs=pl.BlockSpec((tokens, block_rows), lambda i, r, c, g: (0, i)),
        ),
        out_shape=jax.ShapeDtypeStruct((tokens, d_model), jnp.bfloat16),
        interpret=interpret,
    )(tile_rows, tile_cols, own_group, grad_values, gathered, gathered)


def body(layer_input, grad_values, base_weight, tile_ids, tile_delta):
    chips = lax.axis_size("chips")
    n = 2 * chips
    tokens_here = layer_input.shape[0]
    d_model = layer_input.shape[1]
    kv = grad_values.shape[1]
    shard = base_weight.shape[0]
    row_tiles = d_model // TILE
    col_tiles = kv // TILE

    sub = TILE * TILE // kv
    delta_rows = tile_delta.reshape(col_tiles, sub, TILE).transpose(1, 0, 2).reshape(sub, kv)
    groups = lax.axis_size("groups")
    own_group = lax.axis_index("groups")
    half = shard // groups
    mine = lax.dynamic_slice_in_dim(base_weight, own_group * half, half, 0)
    packed = jnp.concatenate([mine, delta_rows], axis=0)
    gathered = lax.all_gather(packed, ("groups",) + DP, axis=0, tiled=False)
    gathered = gathered.reshape(groups, n, half + sub, kv)

    all_ids = lax.all_to_all(jnp.broadcast_to(tile_ids, (n,)), DP, 0, 0, tiled=True)
    tile_rows = all_ids // col_tiles
    tile_cols = all_ids % col_tiles

    input_panels = layer_input.reshape(tokens_here, row_tiles, TILE)
    grad_panels = grad_values.reshape(tokens_here, col_tiles, TILE)
    rows_taken = jnp.take(input_panels, tile_rows, axis=1)
    cols_taken = jnp.take(grad_panels, tile_cols, axis=1)
    partial = jnp.einsum(
        "tja,tjb->jab", rows_taken, cols_taken, preferred_element_type=jnp.float32
    ).reshape(chips, 2, TILE, TILE)
    core = lax.axis_index("core")
    mine = lax.dynamic_index_in_dim(partial, core, axis=1, keepdims=False)
    other = lax.dynamic_index_in_dim(partial, 1 - core, axis=1, keepdims=False)
    chip_sum = mine + lax.ppermute(other, "core", [(0, 1), (1, 0)])
    from_chips = lax.all_to_all(chip_sum, "chips", 0, 0, tiled=True)
    factor = 1.0 / math.sqrt(tokens_here * n)
    grad_tiles = jnp.sum(from_chips, axis=0, keepdims=True) * factor

    group_ids = jnp.reshape(own_group, (1,)).astype(jnp.int32)
    grad_input = merged_matmul(tile_rows, tile_cols, group_ids, grad_values, gathered)
    return (grad_input, grad_tiles)


def solution(mesh):
    groups, dp = mesh.devices.shape
    split = Mesh(mesh.devices.reshape(groups, dp // 2, 2), ("groups",) + DP)
    tokens = ("groups",) + DP
    placed = (
        P(tokens, None),
        P(tokens, None),
        P(DP, None),
        P(tokens),
        P(tokens, None, None),
    )
    return jax.shard_map(
        body,
        mesh=split,
        in_specs=placed,
        out_specs=(P(tokens, None), P(tokens, None, None)),
        check_vma=False,
    )
```

```python
import math

import jax
import jax.numpy as jnp
from jax import lax
from jax.experimental import pallas as pl
from jax.experimental.pallas import tpu as pltpu
from jax.sharding import Mesh
from jax.sharding import PartitionSpec as P

TILE = 128
BLOCK_ROWS = 4096
DP = ("chips", "core")


def merged_matmul(tile_rows, tile_cols, grad_values, gathered, shard, interpret=False):
    tokens, kv = grad_values.shape
    n, packed_rows, _ = gathered.shape
    sub = packed_rows - shard
    d_model = n * shard
    col_tiles = kv // TILE
    block_rows = max(min(BLOCK_ROWS, d_model), shard)
    per_block = block_rows // shard
    tiles_per_block = block_rows // TILE

    def kernel(rows_ref, cols_ref, gv_ref, base_ref, delta_ref, out_ref):
        i = pl.program_id(0)

        def patch(j, carry):
            r = rows_ref[j] - i * tiles_per_block

            @pl.when((r >= 0) & (r < tiles_per_block))
            def _():
                c = cols_ref[j]
                for cc in range(col_tiles):

                    @pl.when(c == cc)
                    def _():
                        cs = slice(cc * TILE, (cc + 1) * TILE)
                        for a in range(col_tiles):
                            at = r * TILE + a * sub
                            si = at // shard
                            rs = pl.ds(pl.multiple_of(at % shard, sub), sub)
                            add = delta_ref[j, :, a * TILE:(a + 1) * TILE].astype(jnp.float32)
                            cur = base_ref[si, rs, cs].astype(jnp.float32)
                            base_ref[si, rs, cs] = (cur + add).astype(jnp.bfloat16)

            return carry

        lax.fori_loop(0, n, patch, 0)
        merged = base_ref[...].reshape(block_rows, kv)
        out_ref[...] = lax.dot_general(
            gv_ref[...],
            merged,
            (((1,), (1,)), ((), ())),
            preferred_element_type=jnp.float32,
        ).astype(out_ref.dtype)

    return pl.pallas_call(
        kernel,
        grid_spec=pltpu.PrefetchScalarGridSpec(
            num_scalar_prefetch=2,
            grid=(d_model // block_rows,),
            in_specs=[
                pl.BlockSpec((tokens, kv), lambda i, r, c: (0, 0)),
                pl.BlockSpec((per_block, shard, kv), lambda i, r, c: (i, 0, 0)),
                pl.BlockSpec((n, sub, kv), lambda i, r, c: (0, shard // sub, 0)),
            ],
            out_specs=pl.BlockSpec((tokens, block_rows), lambda i, r, c: (0, i)),
        ),
        out_shape=jax.ShapeDtypeStruct((tokens, d_model), jnp.bfloat16),
        interpret=interpret,
    )(tile_rows, tile_cols, grad_values, gathered, gathered)


def body(layer_input, grad_values, base_weight, tile_ids, tile_delta):
    chips = lax.axis_size("chips")
    n = 2 * chips
    tokens_here = layer_input.shape[0]
    d_model = layer_input.shape[1]
    kv = grad_values.shape[1]
    shard = base_weight.shape[0]
    row_tiles = d_model // TILE
    col_tiles = kv // TILE

    sub = TILE * TILE // kv
    delta_rows = tile_delta.reshape(col_tiles, sub, TILE).transpose(1, 0, 2).reshape(sub, kv)
    packed = jnp.concatenate([base_weight, delta_rows], axis=0)
    gathered = lax.all_gather(packed, DP, axis=0, tiled=False)

    all_ids = lax.all_to_all(jnp.broadcast_to(tile_ids, (n,)), DP, 0, 0, tiled=True)
    tile_rows = all_ids // col_tiles
    tile_cols = all_ids % col_tiles

    input_panels = layer_input.reshape(tokens_here, row_tiles, TILE)
    grad_panels = grad_values.reshape(tokens_here, col_tiles, TILE)
    rows_taken = jnp.take(input_panels, tile_rows, axis=1)
    cols_taken = jnp.take(grad_panels, tile_cols, axis=1)
    partial = jnp.einsum(
        "tja,tjb->jab", rows_taken, cols_taken, preferred_element_type=jnp.float32
    ).reshape(chips, 2, TILE, TILE)
    core = lax.axis_index("core")
    mine = lax.dynamic_index_in_dim(partial, core, axis=1, keepdims=False)
    other = lax.dynamic_index_in_dim(partial, 1 - core, axis=1, keepdims=False)
    chip_sum = mine + lax.ppermute(other, "core", [(0, 1), (1, 0)])
    from_chips = lax.all_to_all(chip_sum, "chips", 0, 0, tiled=True)
    factor = 1.0 / math.sqrt(tokens_here * n)
    grad_tiles = jnp.sum(from_chips, axis=0, keepdims=True) * factor

    grad_input = merged_matmul(tile_rows, tile_cols, grad_values, gathered, shard)
    return (grad_input, grad_tiles)


def solution(mesh):
    groups, dp = mesh.devices.shape
    split = Mesh(mesh.devices.reshape(groups, dp // 2, 2), ("groups",) + DP)
    tokens = ("groups",) + DP
    placed = (
        P(tokens, None),
        P(tokens, None),
        P(DP, None),
        P(tokens),
        P(tokens, None, None),
    )
    return jax.shard_map(
        body,
        mesh=split,
        in_specs=placed,
        out_specs=(P(tokens, None), P(tokens, None, None)),
        check_vma=False,
    )
```

```python
import math

import jax
import jax.numpy as jnp
from jax import lax
from jax.experimental import pallas as pl
from jax.experimental.pallas import tpu as pltpu
from jax.sharding import Mesh
from jax.sharding import PartitionSpec as P

TILE = 128
BLOCK_ROWS = 4096
DP = ("chips", "core")


def merged_matmul(tile_rows, tile_cols, grad_values, full_base, all_delta_rows, interpret=False):
    tokens, kv = grad_values.shape
    d_model = full_base.shape[0]
    n, sub, _ = all_delta_rows.shape
    col_tiles = kv // TILE
    block_rows = min(BLOCK_ROWS, d_model)
    tiles_per_block = block_rows // TILE

    def kernel(rows_ref, cols_ref, gv_ref, base_ref, delta_ref, out_ref):
        i = pl.program_id(0)

        def patch(j, carry):
            r = rows_ref[j] - i * tiles_per_block

            @pl.when((r >= 0) & (r < tiles_per_block))
            def _():
                c = cols_ref[j]
                for cc in range(col_tiles):

                    @pl.when(c == cc)
                    def _():
                        cs = slice(cc * TILE, (cc + 1) * TILE)
                        for a in range(col_tiles):
                            rs = pl.ds(pl.multiple_of(r * TILE + a * sub, sub), sub)
                            add = delta_ref[j, :, a * TILE:(a + 1) * TILE].astype(jnp.float32)
                            cur = base_ref[rs, cs].astype(jnp.float32)
                            base_ref[rs, cs] = (cur + add).astype(jnp.bfloat16)

            return carry

        lax.fori_loop(0, n, patch, 0)
        out_ref[...] = lax.dot_general(
            gv_ref[...],
            base_ref[...],
            (((1,), (1,)), ((), ())),
            preferred_element_type=jnp.float32,
        ).astype(out_ref.dtype)

    return pl.pallas_call(
        kernel,
        grid_spec=pltpu.PrefetchScalarGridSpec(
            num_scalar_prefetch=2,
            grid=(d_model // block_rows,),
            in_specs=[
                pl.BlockSpec((tokens, kv), lambda i, r, c: (0, 0)),
                pl.BlockSpec((block_rows, kv), lambda i, r, c: (i, 0)),
                pl.BlockSpec((n, sub, kv), lambda i, r, c: (0, 0, 0)),
            ],
            out_specs=pl.BlockSpec((tokens, block_rows), lambda i, r, c: (0, i)),
        ),
        out_shape=jax.ShapeDtypeStruct((tokens, d_model), jnp.bfloat16),
        interpret=interpret,
    )(tile_rows, tile_cols, grad_values, full_base, all_delta_rows)


def body(layer_input, grad_values, base_weight, tile_ids, tile_delta):
    chips = lax.axis_size("chips")
    n = 2 * chips
    tokens_here = layer_input.shape[0]
    d_model = layer_input.shape[1]
    kv = grad_values.shape[1]
    shard = base_weight.shape[0]
    row_tiles = d_model // TILE
    col_tiles = kv // TILE

    sub = TILE * TILE // kv
    delta_rows = tile_delta.reshape(col_tiles, sub, TILE).transpose(1, 0, 2).reshape(sub, kv)
    full_base = lax.all_gather(base_weight, DP, axis=0, tiled=True)
    all_delta_rows = lax.all_gather(delta_rows, DP, axis=0, tiled=False)

    all_ids = lax.all_to_all(jnp.broadcast_to(tile_ids, (n,)), DP, 0, 0, tiled=True)
    tile_rows = all_ids // col_tiles
    tile_cols = all_ids % col_tiles

    input_panels = layer_input.reshape(tokens_here, row_tiles, TILE)
    grad_panels = grad_values.reshape(tokens_here, col_tiles, TILE)
    rows_taken = jnp.take(input_panels, tile_rows, axis=1)
    cols_taken = jnp.take(grad_panels, tile_cols, axis=1)
    partial = jnp.einsum(
        "tja,tjb->jab", rows_taken, cols_taken, preferred_element_type=jnp.float32
    ).reshape(chips, 2, TILE, TILE)
    core = lax.axis_index("core")
    mine = lax.dynamic_index_in_dim(partial, core, axis=1, keepdims=False)
    other = lax.dynamic_index_in_dim(partial, 1 - core, axis=1, keepdims=False)
    chip_sum = mine + lax.ppermute(other, "core", [(0, 1), (1, 0)])
    from_chips = lax.all_to_all(chip_sum, "chips", 0, 0, tiled=True)
    factor = 1.0 / math.sqrt(tokens_here * n)
    grad_tiles = jnp.sum(from_chips, axis=0, keepdims=True) * factor

    grad_input = merged_matmul(tile_rows, tile_cols, grad_values, full_base, all_delta_rows)
    return (grad_input, grad_tiles)


def solution(mesh):
    groups, dp = mesh.devices.shape
    split = Mesh(mesh.devices.reshape(groups, dp // 2, 2), ("groups",) + DP)
    tokens = ("groups",) + DP
    placed = (
        P(tokens, None),
        P(tokens, None),
        P(DP, None),
        P(tokens),
        P(tokens, None, None),
    )
    return jax.shard_map(
        body,
        mesh=split,
        in_specs=placed,
        out_specs=(P(tokens, None), P(tokens, None, None)),
        check_vma=False,
    )
```

```python
import math

import jax
import jax.numpy as jnp
from jax import lax
from jax.experimental import pallas as pl
from jax.experimental.pallas import tpu as pltpu
from jax.sharding import Mesh
from jax.sharding import PartitionSpec as P

TILE = 128
BLOCK_ROWS = 4096
DP = ("chips", "core")


def merged_matmul(tile_rows, tile_cols, grad_values, gathered, shard, interpret=False):
    tokens, kv = grad_values.shape
    n, packed_rows, _ = gathered.shape
    sub = packed_rows - shard
    d_model = n * shard
    col_tiles = kv // TILE
    block_rows = max(min(BLOCK_ROWS, d_model), shard)
    per_block = block_rows // shard
    tiles_per_block = block_rows // TILE

    def kernel(rows_ref, cols_ref, gv_ref, base_ref, delta_ref, out_ref):
        i = pl.program_id(0)

        def patch(j, carry):
            r = rows_ref[j] - i * tiles_per_block

            @pl.when((r >= 0) & (r < tiles_per_block))
            def _():
                c = cols_ref[j]
                for cc in range(col_tiles):

                    @pl.when(c == cc)
                    def _():
                        cs = slice(cc * TILE, (cc + 1) * TILE)
                        for a in range(col_tiles):
                            at = r * TILE + a * sub
                            si = at // shard
                            rs = pl.ds(pl.multiple_of(at % shard, sub), sub)
                            add = delta_ref[j, :, a * TILE:(a + 1) * TILE].astype(jnp.float32)
                            cur = base_ref[si, rs, cs].astype(jnp.float32)
                            base_ref[si, rs, cs] = (cur + add).astype(jnp.bfloat16)

            return carry

        lax.fori_loop(0, n, patch, 0)
        merged = base_ref[...].reshape(block_rows, kv)
        out_ref[...] = lax.dot_general(
            gv_ref[...],
            merged,
            (((1,), (1,)), ((), ())),
            preferred_element_type=jnp.float32,
        ).astype(out_ref.dtype)

    return pl.pallas_call(
        kernel,
        grid_spec=pltpu.PrefetchScalarGridSpec(
            num_scalar_prefetch=2,
            grid=(d_model // block_rows,),
            in_specs=[
                pl.BlockSpec((tokens, kv), lambda i, r, c: (0, 0)),
                pl.BlockSpec((per_block, shard, kv), lambda i, r, c: (i, 0, 0)),
                pl.BlockSpec((n, sub, kv), lambda i, r, c: (0, shard // sub, 0)),
            ],
            out_specs=pl.BlockSpec((tokens, block_rows), lambda i, r, c: (0, i)),
        ),
        out_shape=jax.ShapeDtypeStruct((tokens, d_model), jnp.bfloat16),
        interpret=interpret,
    )(tile_rows, tile_cols, grad_values, gathered, gathered)


def tile_partials(tile_rows, tile_cols, layer_input, grad_values):
    tokens = layer_input.shape[0]
    listed = tile_rows.shape[0]

    def kernel(rows_ref, cols_ref, x_ref, g_ref, o_ref):
        o_ref[0] = jnp.dot(
            x_ref[...].T, g_ref[...], preferred_element_type=jnp.float32
        )

    return pl.pallas_call(
        kernel,
        grid_spec=pltpu.PrefetchScalarGridSpec(
            num_scalar_prefetch=2,
            grid=(listed,),
            in_specs=[
                pl.BlockSpec((tokens, TILE), lambda j, r, c: (0, r[j])),
                pl.BlockSpec((tokens, TILE), lambda j, r, c: (0, c[j])),
            ],
            out_specs=pl.BlockSpec((1, TILE, TILE), lambda j, r, c: (j, 0, 0)),
        ),
        out_shape=jax.ShapeDtypeStruct((listed, TILE, TILE), jnp.float32),
    )(tile_rows, tile_cols, layer_input, grad_values)


def body(layer_input, grad_values, base_weight, tile_ids, tile_delta):
    chips = lax.axis_size("chips")
    n = 2 * chips
    tokens_here = layer_input.shape[0]
    d_model = layer_input.shape[1]
    kv = grad_values.shape[1]
    shard = base_weight.shape[0]
    row_tiles = d_model // TILE
    col_tiles = kv // TILE

    sub = TILE * TILE // kv
    delta_rows = tile_delta.reshape(col_tiles, sub, TILE).transpose(1, 0, 2).reshape(sub, kv)
    packed = jnp.concatenate([base_weight, delta_rows], axis=0)
    gathered = lax.all_gather(packed, DP, axis=0, tiled=False)

    all_ids = lax.all_to_all(jnp.broadcast_to(tile_ids, (n,)), DP, 0, 0, tiled=True)
    tile_rows = all_ids // col_tiles
    tile_cols = all_ids % col_tiles

    partial = tile_partials(tile_rows, tile_cols, layer_input, grad_values)
    partial = partial.reshape(chips, 2, TILE, TILE)
    core = lax.axis_index("core")
    mine = lax.dynamic_index_in_dim(partial, core, axis=1, keepdims=False)
    other = lax.dynamic_index_in_dim(partial, 1 - core, axis=1, keepdims=False)
    chip_sum = mine + lax.ppermute(other, "core", [(0, 1), (1, 0)])
    gathered, chip_sum = lax.optimization_barrier((gathered, chip_sum))
    from_chips = lax.all_to_all(chip_sum, "chips", 0, 0, tiled=True)
    factor = 1.0 / math.sqrt(tokens_here * n)
    grad_tiles = jnp.sum(from_chips, axis=0, keepdims=True) * factor

    grad_input = merged_matmul(tile_rows, tile_cols, grad_values, gathered, shard)
    return (grad_input, grad_tiles)


def solution(mesh):
    groups, dp = mesh.devices.shape
    split = Mesh(mesh.devices.reshape(groups, dp // 2, 2), ("groups",) + DP)
    tokens = ("groups",) + DP
    placed = (
        P(tokens, None),
        P(tokens, None),
        P(DP, None),
        P(tokens),
        P(tokens, None, None),
    )
    return jax.shard_map(
        body,
        mesh=split,
        in_specs=placed,
        out_specs=(P(tokens, None), P(tokens, None, None)),
        check_vma=False,
    )
```

```python
import math

import jax
import jax.numpy as jnp
from jax import lax
from jax.experimental import pallas as pl
from jax.experimental.pallas import tpu as pltpu
from jax.sharding import Mesh
from jax.sharding import PartitionSpec as P

TILE = 128
BLOCK_ROWS = 4096
DP = ("chips", "core")


def merged_matmul(tile_rows, tile_cols, grad_values, gathered, shard, interpret=False):
    tokens, kv = grad_values.shape
    n, packed_rows, _ = gathered.shape
    sub = packed_rows - shard
    d_model = n * shard
    col_tiles = kv // TILE
    block_rows = max(min(BLOCK_ROWS, d_model), shard)
    per_block = block_rows // shard
    tiles_per_block = block_rows // TILE

    def kernel(rows_ref, cols_ref, gv_ref, base_ref, delta_ref, out_ref):
        i = pl.program_id(0)

        def patch(j, carry):
            r = rows_ref[j] - i * tiles_per_block

            @pl.when((r >= 0) & (r < tiles_per_block))
            def _():
                c = cols_ref[j]
                for cc in range(col_tiles):

                    @pl.when(c == cc)
                    def _():
                        cs = slice(cc * TILE, (cc + 1) * TILE)
                        for a in range(col_tiles):
                            at = r * TILE + a * sub
                            si = at // shard
                            rs = pl.ds(pl.multiple_of(at % shard, sub), sub)
                            add = delta_ref[j, :, a * TILE:(a + 1) * TILE].astype(jnp.float32)
                            cur = base_ref[si, rs, cs].astype(jnp.float32)
                            base_ref[si, rs, cs] = (cur + add).astype(jnp.bfloat16)

            return carry

        lax.fori_loop(0, n, patch, 0)
        merged = base_ref[...].reshape(block_rows, kv)
        out_ref[...] = lax.dot_general(
            gv_ref[...],
            merged,
            (((1,), (1,)), ((), ())),
            preferred_element_type=jnp.float32,
        ).astype(out_ref.dtype)

    return pl.pallas_call(
        kernel,
        grid_spec=pltpu.PrefetchScalarGridSpec(
            num_scalar_prefetch=2,
            grid=(d_model // block_rows,),
            in_specs=[
                pl.BlockSpec((tokens, kv), lambda i, r, c: (0, 0)),
                pl.BlockSpec((per_block, shard, kv), lambda i, r, c: (i, 0, 0)),
                pl.BlockSpec((n, sub, kv), lambda i, r, c: (0, shard // sub, 0)),
            ],
            out_specs=pl.BlockSpec((tokens, block_rows), lambda i, r, c: (0, i)),
        ),
        out_shape=jax.ShapeDtypeStruct((tokens, d_model), jnp.bfloat16),
        interpret=interpret,
    )(tile_rows, tile_cols, grad_values, gathered, gathered)


def packed_shard(base_weight, delta_rows):
    rows, kv = base_weight.shape
    sub = delta_rows.shape[0]

    def kernel(b_ref, d_ref, o_ref, sem):
        first = pltpu.make_async_copy(b_ref, o_ref.at[pl.ds(0, rows)], sem.at[0])
        second = pltpu.make_async_copy(d_ref, o_ref.at[pl.ds(rows, sub)], sem.at[1])
        first.start()
        second.start()
        first.wait()
        second.wait()

    return pl.pallas_call(
        kernel,
        in_specs=[pl.BlockSpec(memory_space=pl.ANY), pl.BlockSpec(memory_space=pl.ANY)],
        out_specs=pl.BlockSpec(memory_space=pl.ANY),
        scratch_shapes=[pltpu.SemaphoreType.DMA((2,))],
        out_shape=jax.ShapeDtypeStruct((rows + sub, kv), base_weight.dtype),
    )(base_weight, delta_rows)


def tile_partials(tile_rows, tile_cols, layer_input, grad_values):
    tokens = layer_input.shape[0]
    listed = tile_rows.shape[0]

    def kernel(rows_ref, cols_ref, x_ref, g_ref, o_ref):
        o_ref[0] = jnp.dot(
            x_ref[...].T, g_ref[...], preferred_element_type=jnp.float32
        )

    return pl.pallas_call(
        kernel,
        grid_spec=pltpu.PrefetchScalarGridSpec(
            num_scalar_prefetch=2,
            grid=(listed,),
            in_specs=[
                pl.BlockSpec((tokens, TILE), lambda j, r, c: (0, r[j])),
                pl.BlockSpec((tokens, TILE), lambda j, r, c: (0, c[j])),
            ],
            out_specs=pl.BlockSpec((1, TILE, TILE), lambda j, r, c: (j, 0, 0)),
        ),
        out_shape=jax.ShapeDtypeStruct((listed, TILE, TILE), jnp.float32),
    )(tile_rows, tile_cols, layer_input, grad_values)


def body(layer_input, grad_values, base_weight, tile_ids, tile_delta):
    chips = lax.axis_size("chips")
    n = 2 * chips
    tokens_here = layer_input.shape[0]
    d_model = layer_input.shape[1]
    kv = grad_values.shape[1]
    shard = base_weight.shape[0]
    row_tiles = d_model // TILE
    col_tiles = kv // TILE

    sub = TILE * TILE // kv
    delta_rows = tile_delta.reshape(col_tiles, sub, TILE).transpose(1, 0, 2).reshape(sub, kv)
    packed = packed_shard(base_weight, delta_rows)
    gathered = lax.all_gather(packed, DP, axis=0, tiled=False)

    all_ids = lax.all_to_all(jnp.broadcast_to(tile_ids, (n,)), DP, 0, 0, tiled=True)
    tile_rows = all_ids // col_tiles
    tile_cols = all_ids % col_tiles

    partial = tile_partials(tile_rows, tile_cols, layer_input, grad_values)
    partial = partial.reshape(chips, 2, TILE, TILE)
    core = lax.axis_index("core")
    mine = lax.dynamic_index_in_dim(partial, core, axis=1, keepdims=False)
    other = lax.dynamic_index_in_dim(partial, 1 - core, axis=1, keepdims=False)
    chip_sum = mine + lax.ppermute(other, "core", [(0, 1), (1, 0)])
    gathered, chip_sum = lax.optimization_barrier((gathered, chip_sum))
    from_chips = lax.all_to_all(chip_sum, "chips", 0, 0, tiled=True)
    factor = 1.0 / math.sqrt(tokens_here * n)
    grad_tiles = jnp.sum(from_chips, axis=0, keepdims=True) * factor

    grad_input = merged_matmul(tile_rows, tile_cols, grad_values, gathered, shard)
    return (grad_input, grad_tiles)


def solution(mesh):
    groups, dp = mesh.devices.shape
    split = Mesh(mesh.devices.reshape(groups, dp // 2, 2), ("groups",) + DP)
    tokens = ("groups",) + DP
    placed = (
        P(tokens, None),
        P(tokens, None),
        P(DP, None),
        P(tokens),
        P(tokens, None, None),
    )
    return jax.shard_map(
        body,
        mesh=split,
        in_specs=placed,
        out_specs=(P(tokens, None), P(tokens, None, None)),
        check_vma=False,
    )
```

```python
import math

import jax
import jax.numpy as jnp
from jax import lax
from jax.experimental import pallas as pl
from jax.experimental.pallas import tpu as pltpu
from jax.sharding import Mesh
from jax.sharding import PartitionSpec as P

TILE = 128
BLOCK_ROWS = 4096

DP = ("chips", "core")


def merged_matmul(tile_rows, tile_cols, grad_values, gathered, shard, interpret=False):
    tokens, kv = grad_values.shape
    n, packed_rows, _ = gathered.shape
    sub = packed_rows - shard
    d_model = n * shard
    col_tiles = kv // TILE
    block_rows = max(min(BLOCK_ROWS, d_model), shard)
    per_block = block_rows // shard
    tiles_per_block = block_rows // TILE

    def kernel(rows_ref, cols_ref, gv_ref, base_ref, delta_ref, out_ref):
        i = pl.program_id(0)

        def patch(j, carry):
            r = rows_ref[j] - i * tiles_per_block

            @pl.when((r >= 0) & (r < tiles_per_block))
            def _():
                c = cols_ref[j]
                for cc in range(col_tiles):

                    @pl.when(c == cc)
                    def _():
                        cs = slice(cc * TILE, (cc + 1) * TILE)
                        for a in range(col_tiles):
                            at = r * TILE + a * sub
                            si = at // shard
                            rs = pl.ds(pl.multiple_of(at % shard, sub), sub)
                            add = delta_ref[j, :, a * TILE:(a + 1) * TILE].astype(jnp.float32)
                            cur = base_ref[si, rs, cs].astype(jnp.float32)
                            base_ref[si, rs, cs] = (cur + add).astype(jnp.bfloat16)

            return carry

        lax.fori_loop(0, n, patch, 0)
        merged = base_ref[...].reshape(block_rows, kv)
        out_ref[...] = lax.dot_general(
            gv_ref[...],
            merged,
            (((1,), (1,)), ((), ())),
            preferred_element_type=jnp.float32,
        ).astype(out_ref.dtype)

    return pl.pallas_call(
        kernel,
        grid_spec=pltpu.PrefetchScalarGridSpec(
            num_scalar_prefetch=2,
            grid=(d_model // block_rows,),
            in_specs=[
                pl.BlockSpec((tokens, kv), lambda i, r, c: (0, 0)),
                pl.BlockSpec((per_block, shard, kv), lambda i, r, c: (i, 0, 0)),
                pl.BlockSpec((n, sub, kv), lambda i, r, c: (0, shard // sub, 0)),
            ],
            out_specs=pl.BlockSpec((tokens, block_rows), lambda i, r, c: (0, i)),
        ),
        out_shape=jax.ShapeDtypeStruct((tokens, d_model), jnp.bfloat16),
        interpret=interpret,
    )(tile_rows, tile_cols, grad_values, gathered, gathered)


def tile_partials(tile_rows, tile_cols, layer_input, grad_values):
    tokens = layer_input.shape[0]
    listed = tile_rows.shape[0]

    def kernel(rows_ref, cols_ref, x_ref, g_ref, o_ref):
        o_ref[0] = jnp.dot(
            x_ref[...].T, g_ref[...], preferred_element_type=jnp.float32
        )

    return pl.pallas_call(
        kernel,
        grid_spec=pltpu.PrefetchScalarGridSpec(
            num_scalar_prefetch=2,
            grid=(listed,),
            in_specs=[
                pl.BlockSpec((tokens, TILE), lambda j, r, c: (0, r[j])),
                pl.BlockSpec((tokens, TILE), lambda j, r, c: (0, c[j])),
            ],
            out_specs=pl.BlockSpec((1, TILE, TILE), lambda j, r, c: (j, 0, 0)),
        ),
        out_shape=jax.ShapeDtypeStruct((listed, TILE, TILE), jnp.float32),
    )(tile_rows, tile_cols, layer_input, grad_values)


def body(layer_input, grad_values, base_weight, tile_ids, tile_delta):
    chips = lax.axis_size("chips")
    n = 2 * chips
    tokens_here = layer_input.shape[0]
    d_model = layer_input.shape[1]
    kv = grad_values.shape[1]
    shard = base_weight.shape[0]
    row_tiles = d_model // TILE
    col_tiles = kv // TILE

    sub = TILE * TILE // kv
    delta_rows = tile_delta.reshape(col_tiles, sub, TILE).transpose(1, 0, 2).reshape(sub, kv)
    packed = jnp.concatenate([base_weight, delta_rows], axis=0)
    gathered = lax.all_gather(packed, DP, axis=0, tiled=False)

    all_ids = lax.all_to_all(jnp.broadcast_to(tile_ids, (n,)), DP, 0, 0, tiled=True)
    tile_rows = all_ids // col_tiles
    tile_cols = all_ids % col_tiles

    partial = tile_partials(tile_rows, tile_cols, layer_input, grad_values)
    partial = partial.reshape(chips, 2, TILE, TILE)
    core = lax.axis_index("core")
    mine = lax.dynamic_index_in_dim(partial, core, axis=1, keepdims=False)
    other = lax.dynamic_index_in_dim(partial, 1 - core, axis=1, keepdims=False)
    chip_sum = mine + lax.ppermute(other, "core", [(0, 1), (1, 0)])
    gathered, chip_sum = lax.optimization_barrier((gathered, chip_sum))
    if chips <= 8:
        chip = lax.axis_index("chips")
        summed = lax.dynamic_index_in_dim(chip_sum, chip, axis=0, keepdims=False)
        for shift in range(1, chips):
            send = lax.dynamic_index_in_dim(chip_sum, (chip + shift) % chips, axis=0, keepdims=False)
            ring = [(k, (k + shift) % chips) for k in range(chips)]
            summed = summed + lax.ppermute(send, "chips", ring)
    else:
        from_chips = lax.all_to_all(chip_sum, "chips", 0, 0, tiled=True)
        summed = jnp.sum(from_chips, axis=0)
    factor = 1.0 / math.sqrt(tokens_here * n)
    grad_tiles = summed[None] * factor

    grad_input = merged_matmul(tile_rows, tile_cols, grad_values, gathered, shard)
    return (grad_input, grad_tiles)


def solution(mesh):
    groups, dp = mesh.devices.shape
    split = Mesh(mesh.devices.reshape(groups, dp // 2, 2), ("groups",) + DP)
    tokens = ("groups",) + DP
    placed = (
        P(tokens, None),
        P(tokens, None),
        P(DP, None),
        P(tokens),
        P(tokens, None, None),
    )
    return jax.shard_map(
        body,
        mesh=split,
        in_specs=placed,
        out_specs=(P(tokens, None), P(tokens, None, None)),
        check_vma=False,
    )
```

```python
import math

import jax
import jax.numpy as jnp
from jax import lax
from jax.experimental import pallas as pl
from jax.experimental.pallas import tpu as pltpu
from jax.sharding import Mesh
from jax.sharding import PartitionSpec as P

TILE = 128
CHUNK_ROWS = 512
DP = ("chips", "core")


def merged_matmul(tile_rows, tile_cols, grad_values, gathered, shard):
    tokens, kv = grad_values.shape
    n, packed_rows, _ = gathered.shape
    sub = packed_rows - shard
    d_model = n * shard
    col_tiles = kv // TILE
    chunk_rows = max(CHUNK_ROWS, shard)
    per_chunk = chunk_rows // shard
    chunks = d_model // chunk_rows
    tiles_per_chunk = chunk_rows // TILE

    def kernel(rows_ref, cols_ref, gv_ref, delta_ref, g_hbm, out_hbm, buf, obuf, in_sem, out_sem):
        copies_in = [
            pltpu.make_async_copy(
                g_hbm.at[pl.ds(q * per_chunk, per_chunk), pl.ds(0, shard)],
                buf.at[q],
                in_sem.at[q],
            )
            for q in range(chunks)
        ]
        for cp in copies_in:
            cp.start()
        copies_out = []
        for q in range(chunks):
            copies_in[q].wait()

            def patch(j, carry):
                r = rows_ref[j] - q * tiles_per_chunk

                @pl.when((r >= 0) & (r < tiles_per_chunk))
                def _():
                    c = cols_ref[j]
                    for cc in range(col_tiles):

                        @pl.when(c == cc)
                        def _():
                            cs = slice(cc * TILE, (cc + 1) * TILE)
                            for a in range(col_tiles):
                                at = r * TILE + a * sub
                                si = at // shard
                                rs = pl.ds(pl.multiple_of(at % shard, sub), sub)
                                add = delta_ref[j, :, a * TILE:(a + 1) * TILE].astype(jnp.float32)
                                cur = buf[q, si, rs, cs].astype(jnp.float32)
                                buf[q, si, rs, cs] = (cur + add).astype(jnp.bfloat16)

                return carry

            lax.fori_loop(0, n, patch, 0)
            slot = q % 2
            if q >= 2:
                copies_out[q - 2].wait()
            obuf[slot] = lax.dot_general(
                gv_ref[...],
                buf[q].reshape(chunk_rows, kv),
                (((1,), (1,)), ((), ())),
                preferred_element_type=jnp.float32,
            ).astype(obuf.dtype)
            cp = pltpu.make_async_copy(
                obuf.at[slot],
                out_hbm.at[:, pl.ds(q * chunk_rows, chunk_rows)],
                out_sem.at[slot],
            )
            cp.start()
            copies_out.append(cp)
        for cp in copies_out[-2:]:
            cp.wait()

    return pl.pallas_call(
        kernel,
        grid_spec=pltpu.PrefetchScalarGridSpec(
            num_scalar_prefetch=2,
            grid=(1,),
            in_specs=[
                pl.BlockSpec((tokens, kv), lambda i, r, c: (0, 0)),
                pl.BlockSpec((n, sub, kv), lambda i, r, c: (0, shard // sub, 0)),
                pl.BlockSpec(memory_space=pl.ANY),
            ],
            out_specs=pl.BlockSpec(memory_space=pl.ANY),
            scratch_shapes=[
                pltpu.VMEM((chunks, per_chunk, shard, kv), jnp.bfloat16),
                pltpu.VMEM((2, tokens, chunk_rows), jnp.bfloat16),
                pltpu.SemaphoreType.DMA((chunks,)),
                pltpu.SemaphoreType.DMA((2,)),
            ],
        ),
        out_shape=jax.ShapeDtypeStruct((tokens, d_model), jnp.bfloat16),
        compiler_params=pltpu.CompilerParams(vmem_limit_bytes=56 * 1024 * 1024),
    )(tile_rows, tile_cols, grad_values, gathered, gathered)


def tile_partials(tile_rows, tile_cols, layer_input, grad_values):
    tokens = layer_input.shape[0]
    listed = tile_rows.shape[0]

    def kernel(rows_ref, cols_ref, x_ref, g_ref, o_ref):
        o_ref[0] = jnp.dot(
            x_ref[...].T, g_ref[...], preferred_element_type=jnp.float32
        )

    return pl.pallas_call(
        kernel,
        grid_spec=pltpu.PrefetchScalarGridSpec(
            num_scalar_prefetch=2,
            grid=(listed,),
            in_specs=[
                pl.BlockSpec((tokens, TILE), lambda j, r, c: (0, r[j])),
                pl.BlockSpec((tokens, TILE), lambda j, r, c: (0, c[j])),
            ],
            out_specs=pl.BlockSpec((1, TILE, TILE), lambda j, r, c: (j, 0, 0)),
        ),
        out_shape=jax.ShapeDtypeStruct((listed, TILE, TILE), jnp.float32),
    )(tile_rows, tile_cols, layer_input, grad_values)


def body(layer_input, grad_values, base_weight, tile_ids, tile_delta):
    chips = lax.axis_size("chips")
    n = 2 * chips
    tokens_here = layer_input.shape[0]
    d_model = layer_input.shape[1]
    kv = grad_values.shape[1]
    shard = base_weight.shape[0]
    row_tiles = d_model // TILE
    col_tiles = kv // TILE

    sub = TILE * TILE // kv
    delta_rows = tile_delta.reshape(col_tiles, sub, TILE).transpose(1, 0, 2).reshape(sub, kv)
    packed = jnp.concatenate([base_weight, delta_rows], axis=0)
    gathered = lax.all_gather(packed, DP, axis=0, tiled=False)

    all_ids = lax.all_to_all(jnp.broadcast_to(tile_ids, (n,)), DP, 0, 0, tiled=True)
    tile_rows = all_ids // col_tiles
    tile_cols = all_ids % col_tiles

    partial = tile_partials(tile_rows, tile_cols, layer_input, grad_values)
    partial = partial.reshape(chips, 2, TILE, TILE)
    core = lax.axis_index("core")
    mine = lax.dynamic_index_in_dim(partial, core, axis=1, keepdims=False)
    other = lax.dynamic_index_in_dim(partial, 1 - core, axis=1, keepdims=False)
    chip_sum = mine + lax.ppermute(other, "core", [(0, 1), (1, 0)])
    gathered, chip_sum = lax.optimization_barrier((gathered, chip_sum))
    from_chips = lax.all_to_all(chip_sum, "chips", 0, 0, tiled=True)
    factor = 1.0 / math.sqrt(tokens_here * n)
    grad_tiles = jnp.sum(from_chips, axis=0, keepdims=True) * factor

    grad_input = merged_matmul(tile_rows, tile_cols, grad_values, gathered, shard)
    return (grad_input, grad_tiles)


def solution(mesh):
    groups, dp = mesh.devices.shape
    split = Mesh(mesh.devices.reshape(groups, dp // 2, 2), ("groups",) + DP)
    tokens = ("groups",) + DP
    placed = (
        P(tokens, None),
        P(tokens, None),
        P(DP, None),
        P(tokens),
        P(tokens, None, None),
    )
    return jax.shard_map(
        body,
        mesh=split,
        in_specs=placed,
        out_specs=(P(tokens, None), P(tokens, None, None)),
        check_vma=False,
    )
```

```python
import math

import jax
import jax.numpy as jnp
from jax import lax
from jax.experimental import pallas as pl
from jax.experimental.pallas import tpu as pltpu
from jax.sharding import Mesh
from jax.sharding import PartitionSpec as P

TILE = 128
BLOCK_ROWS = 4096
DP = ("chips", "core")


def merged_matmul(tile_rows, tile_cols, grad_values, gathered, shard, interpret=False):
    tokens, kv = grad_values.shape
    n, packed_rows, _ = gathered.shape
    sub = packed_rows - shard
    d_model = n * shard
    col_tiles = kv // TILE
    block_rows = max(min(BLOCK_ROWS, d_model), shard)
    per_block = block_rows // shard
    tiles_per_block = block_rows // TILE

    def kernel(rows_ref, cols_ref, gv_ref, base_ref, delta_ref, out_ref):
        i = pl.program_id(0)

        def patch(j, carry):
            r = rows_ref[j] - i * tiles_per_block

            @pl.when((r >= 0) & (r < tiles_per_block))
            def _():
                cs = pl.ds(pl.multiple_of(cols_ref[j] * TILE, TILE), TILE)
                for a in range(col_tiles):
                    at = r * TILE + a * sub
                    si = at // shard
                    rs = pl.ds(pl.multiple_of(at % shard, sub), sub)
                    add = delta_ref[j, :, a * TILE:(a + 1) * TILE].astype(jnp.float32)
                    cur = base_ref[si, rs, cs].astype(jnp.float32)
                    base_ref[si, rs, cs] = (cur + add).astype(jnp.bfloat16)

            return carry

        lax.fori_loop(0, n, patch, 0)
        merged = base_ref[...].reshape(block_rows, kv)
        out_ref[...] = lax.dot_general(
            gv_ref[...],
            merged,
            (((1,), (1,)), ((), ())),
            preferred_element_type=jnp.float32,
        ).astype(out_ref.dtype)

    return pl.pallas_call(
        kernel,
        grid_spec=pltpu.PrefetchScalarGridSpec(
            num_scalar_prefetch=2,
            grid=(d_model // block_rows,),
            in_specs=[
                pl.BlockSpec((tokens, kv), lambda i, r, c: (0, 0)),
                pl.BlockSpec((per_block, shard, kv), lambda i, r, c: (i, 0, 0)),
                pl.BlockSpec((n, sub, kv), lambda i, r, c: (0, shard // sub, 0)),
            ],
            out_specs=pl.BlockSpec((tokens, block_rows), lambda i, r, c: (0, i)),
        ),
        out_shape=jax.ShapeDtypeStruct((tokens, d_model), jnp.bfloat16),
        interpret=interpret,
    )(tile_rows, tile_cols, grad_values, gathered, gathered)


def tile_partials(tile_rows, tile_cols, layer_input, grad_values):
    tokens = layer_input.shape[0]
    listed = tile_rows.shape[0]

    def kernel(rows_ref, cols_ref, x_ref, g_ref, o_ref):
        o_ref[0] = jnp.dot(
            x_ref[...].T, g_ref[...], preferred_element_type=jnp.float32
        )

    return pl.pallas_call(
        kernel,
        grid_spec=pltpu.PrefetchScalarGridSpec(
            num_scalar_prefetch=2,
            grid=(listed,),
            in_specs=[
                pl.BlockSpec((tokens, TILE), lambda j, r, c: (0, r[j])),
                pl.BlockSpec((tokens, TILE), lambda j, r, c: (0, c[j])),
            ],
            out_specs=pl.BlockSpec((1, TILE, TILE), lambda j, r, c: (j, 0, 0)),
        ),
        out_shape=jax.ShapeDtypeStruct((listed, TILE, TILE), jnp.float32),
    )(tile_rows, tile_cols, layer_input, grad_values)


def body(layer_input, grad_values, base_weight, tile_ids, tile_delta):
    chips = lax.axis_size("chips")
    n = 2 * chips
    tokens_here = layer_input.shape[0]
    d_model = layer_input.shape[1]
    kv = grad_values.shape[1]
    shard = base_weight.shape[0]
    row_tiles = d_model // TILE
    col_tiles = kv // TILE

    sub = TILE * TILE // kv
    delta_rows = tile_delta.reshape(col_tiles, sub, TILE).transpose(1, 0, 2).reshape(sub, kv)
    packed = jnp.concatenate([base_weight, delta_rows], axis=0)
    gathered = lax.all_gather(packed, DP, axis=0, tiled=False)

    all_ids = lax.all_to_all(jnp.broadcast_to(tile_ids, (n,)), DP, 0, 0, tiled=True)
    tile_rows = all_ids // col_tiles
    tile_cols = all_ids % col_tiles

    partial = tile_partials(tile_rows, tile_cols, layer_input, grad_values)
    partial = partial.reshape(chips, 2, TILE, TILE)
    core = lax.axis_index("core")
    mine = lax.dynamic_index_in_dim(partial, core, axis=1, keepdims=False)
    other = lax.dynamic_index_in_dim(partial, 1 - core, axis=1, keepdims=False)
    chip_sum = mine + lax.ppermute(other, "core", [(0, 1), (1, 0)])
    gathered, chip_sum = lax.optimization_barrier((gathered, chip_sum))
    from_chips = lax.all_to_all(chip_sum, "chips", 0, 0, tiled=True)
    factor = 1.0 / math.sqrt(tokens_here * n)
    grad_tiles = jnp.sum(from_chips, axis=0, keepdims=True) * factor

    grad_input = merged_matmul(tile_rows, tile_cols, grad_values, gathered, shard)
    return (grad_input, grad_tiles)


def solution(mesh):
    groups, dp = mesh.devices.shape
    split = Mesh(mesh.devices.reshape(groups, dp // 2, 2), ("groups",) + DP)
    tokens = ("groups",) + DP
    placed = (
        P(tokens, None),
        P(tokens, None),
        P(DP, None),
        P(tokens),
        P(tokens, None, None),
    )
    return jax.shard_map(
        body,
        mesh=split,
        in_specs=placed,
        out_specs=(P(tokens, None), P(tokens, None, None)),
        check_vma=False,
    )
```

```python
import math

import jax
import jax.numpy as jnp
from jax import lax
from jax.experimental import pallas as pl
from jax.experimental.pallas import tpu as pltpu
from jax.sharding import Mesh
from jax.sharding import PartitionSpec as P

TILE = 128
BLOCK_ROWS = 4096
DP = ("chips", "core")


def merged_matmul(tile_rows, tile_cols, grad_values, gathered, shard, interpret=False):
    tokens, kv = grad_values.shape
    n, packed_rows, _ = gathered.shape
    sub = packed_rows - shard
    d_model = n * shard
    col_tiles = kv // TILE
    block_rows = max(min(BLOCK_ROWS, d_model), shard)
    per_block = block_rows // shard
    tiles_per_block = block_rows // TILE

    def kernel(rows_ref, cols_ref, gv_ref, base_ref, delta_ref, out_ref):
        i = pl.program_id(0)

        def patch(j, carry):
            r = rows_ref[j] - i * tiles_per_block

            @pl.when((r >= 0) & (r < tiles_per_block))
            def _():
                cs = pl.ds(pl.multiple_of(cols_ref[j] * TILE, TILE), TILE)
                for a in range(col_tiles):
                    at = r * TILE + a * sub
                    si = at // shard
                    rs = pl.ds(pl.multiple_of(at % shard, sub), sub)
                    add = delta_ref[j, :, a * TILE:(a + 1) * TILE].astype(jnp.float32)
                    cur = base_ref[si, rs, cs].astype(jnp.float32)
                    base_ref[si, rs, cs] = (cur + add).astype(jnp.bfloat16)

            return carry

        lax.fori_loop(0, n, patch, 0)
        merged = base_ref[...].reshape(block_rows, kv)
        out_ref[...] = lax.dot_general(
            gv_ref[...],
            merged,
            (((1,), (1,)), ((), ())),
            preferred_element_type=jnp.float32,
        ).astype(out_ref.dtype)

    return pl.pallas_call(
        kernel,
        grid_spec=pltpu.PrefetchScalarGridSpec(
            num_scalar_prefetch=2,
            grid=(d_model // block_rows,),
            in_specs=[
                pl.BlockSpec((tokens, kv), lambda i, r, c: (0, 0)),
                pl.BlockSpec((per_block, shard, kv), lambda i, r, c: (i, 0, 0)),
                pl.BlockSpec((n, sub, kv), lambda i, r, c: (0, shard // sub, 0)),
            ],
            out_specs=pl.BlockSpec((tokens, block_rows), lambda i, r, c: (0, i)),
        ),
        out_shape=jax.ShapeDtypeStruct((tokens, d_model), jnp.bfloat16),
        interpret=interpret,
    )(tile_rows, tile_cols, grad_values, gathered, gathered)


def packed_shard(base_weight, tile_delta):
    rows, kv = base_weight.shape
    col_tiles = kv // TILE
    sub = TILE * TILE // kv

    def kernel(b_ref, d_ref, o_ref):
        o_ref[:rows, :] = b_ref[...]
        for a in range(col_tiles):
            o_ref[rows:, a * TILE:(a + 1) * TILE] = d_ref[0, a * sub:(a + 1) * sub, :]

    return pl.pallas_call(
        kernel,
        out_shape=jax.ShapeDtypeStruct((rows + sub, kv), base_weight.dtype),
    )(base_weight, tile_delta)


def tile_partials(tile_rows, tile_cols, layer_input, grad_values):
    tokens = layer_input.shape[0]
    listed = tile_rows.shape[0]

    def kernel(rows_ref, cols_ref, x_ref, g_ref, o_ref):
        o_ref[0] = jnp.dot(
            x_ref[...].T, g_ref[...], preferred_element_type=jnp.float32
        )

    return pl.pallas_call(
        kernel,
        grid_spec=pltpu.PrefetchScalarGridSpec(
            num_scalar_prefetch=2,
            grid=(listed,),
            in_specs=[
                pl.BlockSpec((tokens, TILE), lambda j, r, c: (0, r[j])),
                pl.BlockSpec((tokens, TILE), lambda j, r, c: (0, c[j])),
            ],
            out_specs=pl.BlockSpec((1, TILE, TILE), lambda j, r, c: (j, 0, 0)),
        ),
        out_shape=jax.ShapeDtypeStruct((listed, TILE, TILE), jnp.float32),
    )(tile_rows, tile_cols, layer_input, grad_values)


def body(layer_input, grad_values, base_weight, tile_ids, tile_delta):
    chips = lax.axis_size("chips")
    n = 2 * chips
    tokens_here = layer_input.shape[0]
    d_model = layer_input.shape[1]
    kv = grad_values.shape[1]
    shard = base_weight.shape[0]
    row_tiles = d_model // TILE
    col_tiles = kv // TILE

    packed = packed_shard(base_weight, tile_delta)
    gathered = lax.all_gather(packed, DP, axis=0, tiled=False)

    all_ids = lax.all_to_all(jnp.broadcast_to(tile_ids, (n,)), DP, 0, 0, tiled=True)
    tile_rows = all_ids // col_tiles
    tile_cols = all_ids % col_tiles

    partial = tile_partials(tile_rows, tile_cols, layer_input, grad_values)
    partial = partial.reshape(chips, 2, TILE, TILE)
    core = lax.axis_index("core")
    mine = lax.dynamic_index_in_dim(partial, core, axis=1, keepdims=False)
    other = lax.dynamic_index_in_dim(partial, 1 - core, axis=1, keepdims=False)
    chip_sum = mine + lax.ppermute(other, "core", [(0, 1), (1, 0)])
    gathered, chip_sum = lax.optimization_barrier((gathered, chip_sum))
    from_chips = lax.all_to_all(chip_sum, "chips", 0, 0, tiled=True)
    factor = 1.0 / math.sqrt(tokens_here * n)
    grad_tiles = jnp.sum(from_chips, axis=0, keepdims=True) * factor

    grad_input = merged_matmul(tile_rows, tile_cols, grad_values, gathered, shard)
    return (grad_input, grad_tiles)


def solution(mesh):
    groups, dp = mesh.devices.shape
    split = Mesh(mesh.devices.reshape(groups, dp // 2, 2), ("groups",) + DP)
    tokens = ("groups",) + DP
    placed = (
        P(tokens, None),
        P(tokens, None),
        P(DP, None),
        P(tokens),
        P(tokens, None, None),
    )
    return jax.shard_map(
        body,
        mesh=split,
        in_specs=placed,
        out_specs=(P(tokens, None), P(tokens, None, None)),
        check_vma=False,
    )
```

```python
import math

import jax
import jax.numpy as jnp
from jax import lax
from jax.experimental import pallas as pl
from jax.experimental.pallas import tpu as pltpu
from jax.sharding import Mesh
from jax.sharding import PartitionSpec as P

TILE = 128
BLOCK_ROWS = 4096
DP = ("za", "zb", "core")


def merged_matmul(tile_rows, tile_cols, grad_values, gathered, shard, interpret=False):
    tokens, kv = grad_values.shape
    n, packed_rows, _ = gathered.shape
    sub = packed_rows - shard
    d_model = n * shard
    col_tiles = kv // TILE
    block_rows = max(min(BLOCK_ROWS, d_model), shard)
    per_block = block_rows // shard
    tiles_per_block = block_rows // TILE

    def kernel(rows_ref, cols_ref, gv_ref, base_ref, delta_ref, out_ref):
        i = pl.program_id(0)

        def patch(j, carry):
            r = rows_ref[j] - i * tiles_per_block

            @pl.when((r >= 0) & (r < tiles_per_block))
            def _():
                cs = pl.ds(pl.multiple_of(cols_ref[j] * TILE, TILE), TILE)
                for a in range(col_tiles):
                    at = r * TILE + a * sub
                    si = at // shard
                    rs = pl.ds(pl.multiple_of(at % shard, sub), sub)
                    add = delta_ref[j, :, a * TILE:(a + 1) * TILE].astype(jnp.float32)
                    cur = base_ref[si, rs, cs].astype(jnp.float32)
                    base_ref[si, rs, cs] = (cur + add).astype(jnp.bfloat16)

            return carry

        lax.fori_loop(0, n, patch, 0)
        merged = base_ref[...].reshape(block_rows, kv)
        out_ref[...] = lax.dot_general(
            gv_ref[...],
            merged,
            (((1,), (1,)), ((), ())),
            preferred_element_type=jnp.float32,
        ).astype(out_ref.dtype)

    return pl.pallas_call(
        kernel,
        grid_spec=pltpu.PrefetchScalarGridSpec(
            num_scalar_prefetch=2,
            grid=(d_model // block_rows,),
            in_specs=[
                pl.BlockSpec((tokens, kv), lambda i, r, c: (0, 0)),
                pl.BlockSpec((per_block, shard, kv), lambda i, r, c: (i, 0, 0)),
                pl.BlockSpec((n, sub, kv), lambda i, r, c: (0, shard // sub, 0)),
            ],
            out_specs=pl.BlockSpec((tokens, block_rows), lambda i, r, c: (0, i)),
        ),
        out_shape=jax.ShapeDtypeStruct((tokens, d_model), jnp.bfloat16),
        interpret=interpret,
    )(tile_rows, tile_cols, grad_values, gathered, gathered)


def packed_shard(base_weight, tile_delta):
    rows, kv = base_weight.shape
    col_tiles = kv // TILE
    sub = TILE * TILE // kv

    def kernel(b_ref, d_ref, o_ref):
        o_ref[:rows, :] = b_ref[...]
        for a in range(col_tiles):
            o_ref[rows:, a * TILE:(a + 1) * TILE] = d_ref[0, a * sub:(a + 1) * sub, :]

    return pl.pallas_call(
        kernel,
        out_shape=jax.ShapeDtypeStruct((rows + sub, kv), base_weight.dtype),
    )(base_weight, tile_delta)


def tile_partials(tile_rows, tile_cols, layer_input, grad_values):
    tokens = layer_input.shape[0]
    listed = tile_rows.shape[0]

    def kernel(rows_ref, cols_ref, x_ref, g_ref, o_ref):
        o_ref[0] = jnp.dot(
            x_ref[...].T, g_ref[...], preferred_element_type=jnp.float32
        )

    return pl.pallas_call(
        kernel,
        grid_spec=pltpu.PrefetchScalarGridSpec(
            num_scalar_prefetch=2,
            grid=(listed,),
            in_specs=[
                pl.BlockSpec((tokens, TILE), lambda j, r, c: (0, r[j])),
                pl.BlockSpec((tokens, TILE), lambda j, r, c: (0, c[j])),
            ],
            out_specs=pl.BlockSpec((1, TILE, TILE), lambda j, r, c: (j, 0, 0)),
        ),
        out_shape=jax.ShapeDtypeStruct((listed, TILE, TILE), jnp.float32),
    )(tile_rows, tile_cols, layer_input, grad_values)


def body(layer_input, grad_values, base_weight, tile_ids, tile_delta):
    outer = lax.axis_size("za")
    inner = lax.axis_size("zb")
    chips = outer * inner
    n = 2 * chips
    tokens_here = layer_input.shape[0]
    d_model = layer_input.shape[1]
    kv = grad_values.shape[1]
    shard = base_weight.shape[0]
    row_tiles = d_model // TILE
    col_tiles = kv // TILE

    packed = packed_shard(base_weight, tile_delta)
    gathered = lax.all_gather(packed, DP, axis=0, tiled=False)

    all_ids = lax.all_to_all(jnp.broadcast_to(tile_ids, (n,)), DP, 0, 0, tiled=True)
    tile_rows = all_ids // col_tiles
    tile_cols = all_ids % col_tiles

    partial = tile_partials(tile_rows, tile_cols, layer_input, grad_values)
    partial = partial.reshape(chips, 2, TILE, TILE)
    core = lax.axis_index("core")
    mine = lax.dynamic_index_in_dim(partial, core, axis=1, keepdims=False)
    other = lax.dynamic_index_in_dim(partial, 1 - core, axis=1, keepdims=False)
    chip_sum = mine + lax.ppermute(other, "core", [(0, 1), (1, 0)])
    if inner == 2:
        pair = chip_sum.reshape(outer, inner, TILE, TILE)
        at = lax.axis_index("zb")
        keep = lax.dynamic_index_in_dim(pair, at, axis=1, keepdims=False)
        give = lax.dynamic_index_in_dim(pair, 1 - at, axis=1, keepdims=False)
        chip_sum = keep + lax.ppermute(give, "zb", [(0, 1), (1, 0)])
        across = "za"
    else:
        across = ("za", "zb")
    gathered, chip_sum = lax.optimization_barrier((gathered, chip_sum))
    from_chips = lax.all_to_all(chip_sum, across, 0, 0, tiled=True)
    factor = 1.0 / math.sqrt(tokens_here * n)
    grad_tiles = jnp.sum(from_chips, axis=0, keepdims=True) * factor

    grad_input = merged_matmul(tile_rows, tile_cols, grad_values, gathered, shard)
    return (grad_input, grad_tiles)


def solution(mesh):
    groups, dp = mesh.devices.shape
    seq = list(mesh.devices[0][::2])
    changes = [sum(a.coords[i] != b.coords[i] for a, b in zip(seq, seq[1:])) for i in range(3)]
    slowest = min((c, i) for i, c in enumerate(changes) if c > 0)[1]
    inner = len(seq) // (changes[slowest] + 1)
    split = Mesh(mesh.devices.reshape(groups, dp // 2 // inner, inner, 2), ("groups",) + DP)
    tokens = ("groups",) + DP
    placed = (
        P(tokens, None),
        P(tokens, None),
        P(DP, None),
        P(tokens),
        P(tokens, None, None),
    )
    return jax.shard_map(
        body,
        mesh=split,
        in_specs=placed,
        out_specs=(P(tokens, None), P(tokens, None, None)),
        check_vma=False,
    )
```

```python
import math

import jax
import jax.numpy as jnp
from jax import lax
from jax.experimental import pallas as pl
from jax.experimental.pallas import tpu as pltpu
from jax.sharding import Mesh
from jax.sharding import PartitionSpec as P

TILE = 128
BLOCK_ROWS = 4096
DP = ("chips", "core")


def merged_matmul(tile_rows, tile_cols, grad_values, gathered, shard, interpret=False):
    tokens, kv = grad_values.shape
    n, packed_rows, _ = gathered.shape
    sub = packed_rows - shard
    d_model = n * shard
    col_tiles = kv // TILE
    block_rows = max(min(BLOCK_ROWS, d_model), shard)
    per_block = block_rows // shard
    tiles_per_block = block_rows // TILE

    def kernel(rows_ref, cols_ref, gv_ref, base_ref, delta_ref, out_ref):
        i = pl.program_id(0)

        def patch(j, carry):
            r = rows_ref[j] - i * tiles_per_block

            @pl.when((r >= 0) & (r < tiles_per_block))
            def _():
                cs = pl.ds(pl.multiple_of(cols_ref[j] * TILE, TILE), TILE)
                for a in range(col_tiles):
                    at = r * TILE + a * sub
                    si = at // shard
                    rs = pl.ds(pl.multiple_of(at % shard, sub), sub)
                    add = delta_ref[j, :, a * TILE:(a + 1) * TILE].astype(jnp.float32)
                    cur = base_ref[si, rs, cs].astype(jnp.float32)
                    base_ref[si, rs, cs] = (cur + add).astype(jnp.bfloat16)

            return carry

        lax.fori_loop(0, n, patch, 0)
        merged = base_ref[...].reshape(block_rows, kv)
        out_ref[...] = lax.dot_general(
            gv_ref[...],
            merged,
            (((1,), (1,)), ((), ())),
            preferred_element_type=jnp.float32,
        ).astype(out_ref.dtype)

    return pl.pallas_call(
        kernel,
        grid_spec=pltpu.PrefetchScalarGridSpec(
            num_scalar_prefetch=2,
            grid=(d_model // block_rows,),
            in_specs=[
                pl.BlockSpec((tokens, kv), lambda i, r, c: (0, 0)),
                pl.BlockSpec((per_block, shard, kv), lambda i, r, c: (i, 0, 0)),
                pl.BlockSpec((n, sub, kv), lambda i, r, c: (0, shard // sub, 0)),
            ],
            out_specs=pl.BlockSpec((tokens, block_rows), lambda i, r, c: (0, i)),
        ),
        out_shape=jax.ShapeDtypeStruct((tokens, d_model), jnp.bfloat16),
        interpret=interpret,
    )(tile_rows, tile_cols, grad_values, gathered, gathered)


def packed_shard(base_weight, tile_delta):
    rows, kv = base_weight.shape
    col_tiles = kv // TILE
    sub = TILE * TILE // kv
    total = rows + sub
    steps = 3 if total % 3 == 0 and (total // 3) % sub == 0 and total // 3 >= sub else 1
    block = total // steps
    last = rows - (steps - 1) * block

    def kernel(b_ref, d_ref, o_ref):
        i = pl.program_id(0)

        @pl.when(i < steps - 1)
        def _():
            o_ref[...] = b_ref[...]

        @pl.when(i == steps - 1)
        def _():
            o_ref[:last, :] = b_ref[:last, :]
            for a in range(col_tiles):
                o_ref[last:, a * TILE:(a + 1) * TILE] = d_ref[0, a * sub:(a + 1) * sub, :]

    return pl.pallas_call(
        kernel,
        grid=(steps,),
        in_specs=[
            pl.BlockSpec((block, kv), lambda i: (i, 0)),
            pl.BlockSpec((1, TILE, TILE), lambda i: (0, 0, 0)),
        ],
        out_specs=pl.BlockSpec((block, kv), lambda i: (i, 0)),
        out_shape=jax.ShapeDtypeStruct((total, kv), base_weight.dtype),
    )(base_weight, tile_delta)


def tile_partials(tile_rows, tile_cols, layer_input, grad_values):
    tokens = layer_input.shape[0]
    listed = tile_rows.shape[0]

    def kernel(rows_ref, cols_ref, x_ref, g_ref, o_ref):
        o_ref[0] = jnp.dot(
            x_ref[...].T, g_ref[...], preferred_element_type=jnp.float32
        )

    return pl.pallas_call(
        kernel,
        grid_spec=pltpu.PrefetchScalarGridSpec(
            num_scalar_prefetch=2,
            grid=(listed,),
            in_specs=[
                pl.BlockSpec((tokens, TILE), lambda j, r, c: (0, r[j])),
                pl.BlockSpec((tokens, TILE), lambda j, r, c: (0, c[j])),
            ],
            out_specs=pl.BlockSpec((1, TILE, TILE), lambda j, r, c: (j, 0, 0)),
        ),
        out_shape=jax.ShapeDtypeStruct((listed, TILE, TILE), jnp.float32),
    )(tile_rows, tile_cols, layer_input, grad_values)


def body(layer_input, grad_values, base_weight, tile_ids, tile_delta):
    chips = lax.axis_size("chips")
    n = 2 * chips
    tokens_here = layer_input.shape[0]
    d_model = layer_input.shape[1]
    kv = grad_values.shape[1]
    shard = base_weight.shape[0]
    row_tiles = d_model // TILE
    col_tiles = kv // TILE

    packed = packed_shard(base_weight, tile_delta)
    gathered = lax.all_gather(packed, DP, axis=0, tiled=False)

    all_ids = lax.all_to_all(jnp.broadcast_to(tile_ids, (n,)), DP, 0, 0, tiled=True)
    tile_rows = all_ids // col_tiles
    tile_cols = all_ids % col_tiles

    partial = tile_partials(tile_rows, tile_cols, layer_input, grad_values)
    partial = partial.reshape(chips, 2, TILE, TILE)
    core = lax.axis_index("core")
    mine = lax.dynamic_index_in_dim(partial, core, axis=1, keepdims=False)
    other = lax.dynamic_index_in_dim(partial, 1 - core, axis=1, keepdims=False)
    chip_sum = mine + lax.ppermute(other, "core", [(0, 1), (1, 0)])
    gathered, chip_sum = lax.optimization_barrier((gathered, chip_sum))
    from_chips = lax.all_to_all(chip_sum, "chips", 0, 0, tiled=True)
    factor = 1.0 / math.sqrt(tokens_here * n)
    grad_tiles = jnp.sum(from_chips, axis=0, keepdims=True) * factor

    grad_input = merged_matmul(tile_rows, tile_cols, grad_values, gathered, shard)
    return (grad_input, grad_tiles)


def solution(mesh):
    groups, dp = mesh.devices.shape
    split = Mesh(mesh.devices.reshape(groups, dp // 2, 2), ("groups",) + DP)
    tokens = ("groups",) + DP
    placed = (
        P(tokens, None),
        P(tokens, None),
        P(DP, None),
        P(tokens),
        P(tokens, None, None),
    )
    return jax.shard_map(
        body,
        mesh=split,
        in_specs=placed,
        out_specs=(P(tokens, None), P(tokens, None, None)),
        check_vma=False,
    )
```

```python
import math

import jax
import jax.numpy as jnp
from jax import lax
from jax.experimental import pallas as pl
from jax.experimental.pallas import tpu as pltpu
from jax.sharding import Mesh
from jax.sharding import PartitionSpec as P

TILE = 128
BLOCK_ROWS = 4096
DP = ("chips", "core")


def merged_matmul(tile_rows, tile_cols, grad_values, gathered, shard, interpret=False):
    tokens, kv = grad_values.shape
    n, packed_rows, _ = gathered.shape
    sub = packed_rows - shard
    d_model = n * shard
    col_tiles = kv // TILE
    block_rows = max(min(BLOCK_ROWS, d_model), shard)
    per_block = block_rows // shard
    tiles_per_block = block_rows // TILE

    def kernel(rows_ref, cols_ref, gv_ref, base_ref, delta_ref, out_ref):
        i = pl.program_id(0)

        def patch(j, carry):
            r = rows_ref[j] - i * tiles_per_block

            @pl.when((r >= 0) & (r < tiles_per_block))
            def _():
                cs = pl.ds(pl.multiple_of(cols_ref[j] * TILE, TILE), TILE)
                for a in range(col_tiles):
                    at = r * TILE + a * sub
                    si = at // shard
                    rs = pl.ds(pl.multiple_of(at % shard, sub), sub)
                    add = delta_ref[j, :, a * TILE:(a + 1) * TILE].astype(jnp.float32)
                    cur = base_ref[si, rs, cs].astype(jnp.float32)
                    base_ref[si, rs, cs] = (cur + add).astype(jnp.bfloat16)

            return carry

        lax.fori_loop(0, n, patch, 0)
        merged = base_ref[...].reshape(block_rows, kv)
        out_ref[...] = lax.dot_general(
            gv_ref[...],
            merged,
            (((1,), (1,)), ((), ())),
            preferred_element_type=jnp.float32,
        ).astype(out_ref.dtype)

    return pl.pallas_call(
        kernel,
        grid_spec=pltpu.PrefetchScalarGridSpec(
            num_scalar_prefetch=2,
            grid=(d_model // block_rows,),
            in_specs=[
                pl.BlockSpec((tokens, kv), lambda i, r, c: (0, 0)),
                pl.BlockSpec((per_block, shard, kv), lambda i, r, c: (i, 0, 0)),
                pl.BlockSpec((n, sub, kv), lambda i, r, c: (0, shard // sub, 0)),
            ],
            out_specs=pl.BlockSpec((tokens, block_rows), lambda i, r, c: (0, i)),
        ),
        out_shape=jax.ShapeDtypeStruct((tokens, d_model), jnp.bfloat16),
        interpret=interpret,
    )(tile_rows, tile_cols, grad_values, gathered, gathered)


def packed_shard(base_weight, tile_delta):
    rows, kv = base_weight.shape
    col_tiles = kv // TILE
    sub = TILE * TILE // kv

    def kernel(b_ref, d_ref, o_ref):
        o_ref[:rows, :] = b_ref[...]
        for a in range(col_tiles):
            o_ref[rows:, a * TILE:(a + 1) * TILE] = d_ref[0, a * sub:(a + 1) * sub, :]

    return pl.pallas_call(
        kernel,
        out_shape=jax.ShapeDtypeStruct((rows + sub, kv), base_weight.dtype),
    )(base_weight, tile_delta)


def tile_partials(tile_rows, tile_cols, layer_input, grad_values):
    tokens = layer_input.shape[0]
    listed = tile_rows.shape[0]

    def kernel(rows_ref, cols_ref, x_ref, g_ref, o_ref):
        o_ref[0] = jnp.dot(
            x_ref[...].T, g_ref[...], preferred_element_type=jnp.float32
        )

    return pl.pallas_call(
        kernel,
        grid_spec=pltpu.PrefetchScalarGridSpec(
            num_scalar_prefetch=2,
            grid=(listed,),
            in_specs=[
                pl.BlockSpec((tokens, TILE), lambda j, r, c: (0, r[j])),
                pl.BlockSpec((tokens, TILE), lambda j, r, c: (0, c[j])),
            ],
            out_specs=pl.BlockSpec((1, TILE, TILE), lambda j, r, c: (j, 0, 0)),
        ),
        out_shape=jax.ShapeDtypeStruct((listed, TILE, TILE), jnp.float32),
    )(tile_rows, tile_cols, layer_input, grad_values)


def body(layer_input, grad_values, base_weight, tile_ids, tile_delta):
    chips = lax.axis_size("chips")
    n = 2 * chips
    tokens_here = layer_input.shape[0]
    d_model = layer_input.shape[1]
    kv = grad_values.shape[1]
    shard = base_weight.shape[0]
    row_tiles = d_model // TILE
    col_tiles = kv // TILE

    packed = packed_shard(base_weight, tile_delta)
    gathered = lax.all_gather(packed, DP, axis=0, tiled=False)

    all_ids = lax.all_to_all(jnp.broadcast_to(tile_ids, (n,)), DP, 0, 0, tiled=True)
    tile_rows = all_ids // col_tiles
    tile_cols = all_ids % col_tiles

    partial = tile_partials(tile_rows, tile_cols, layer_input, grad_values)
    partial = partial.reshape(chips, 2, TILE, TILE)
    core = lax.axis_index("core")
    mine = lax.dynamic_index_in_dim(partial, core, axis=1, keepdims=False)
    other = lax.dynamic_index_in_dim(partial, 1 - core, axis=1, keepdims=False)
    chip_sum = mine + lax.ppermute(other, "core", [(0, 1), (1, 0)])
    gathered, chip_sum = lax.optimization_barrier((gathered, chip_sum))
    flat = chip_sum.reshape(chips, TILE * TILE)
    from_chips = lax.all_to_all(flat, "chips", 0, 0, tiled=True)
    factor = 1.0 / math.sqrt(tokens_here * n)
    grad_tiles = jnp.sum(from_chips, axis=0).reshape(1, TILE, TILE) * factor

    grad_input = merged_matmul(tile_rows, tile_cols, grad_values, gathered, shard)
    return (grad_input, grad_tiles)


def solution(mesh):
    groups, dp = mesh.devices.shape
    split = Mesh(mesh.devices.reshape(groups, dp // 2, 2), ("groups",) + DP)
    tokens = ("groups",) + DP
    placed = (
        P(tokens, None),
        P(tokens, None),
        P(DP, None),
        P(tokens),
        P(tokens, None, None),
    )
    return jax.shard_map(
        body,
        mesh=split,
        in_specs=placed,
        out_specs=(P(tokens, None), P(tokens, None, None)),
        check_vma=False,
    )
```
